128 devices in a mesh: segment: 4 (over z), latent: 8 (over y_hi, x), tok: 4 (over y_lo, core).
Axes of the slice: x: 4, y: 4 (y_hi: 2, y_lo: 2; y = y_hi * 2 + y_lo), z: 4, core: 2. Of those that a mesh axis runs over, the one named last changes fastest.
Arguments:
- window: bfloat16 [512, 2304], P('tok'), may hold values from -8 to 8
- norm_gain: float32 [4, 2304], P('segment'), may hold values from 0.25 to 1.75
- enc_weight: bfloat16 [4, 2304, 65536], P('segment', None, ('latent', 'tok')), may hold values from -0.125 to 0.125
- enc_bias: float32 [4, 65536], P('segment', ('latent', 'tok')), may hold values from -1.5 to 1.5
- thresholds: int32 [4, 65536], P('segment', ('latent', 'tok')), may hold values from 256 to 1535
- dec_weight: bfloat16 [4, 65536, 2304], P('segment', ('latent', 'tok')), may hold values from -0.046875 to 0.046875
- dec_bias: float32 [4, 2304], P('segment'), may hold values from -2.5 to 2.5
- rates_start: float32 [4, 65536], P('segment', ('latent', 'tok')), may hold values from 0 to 1
- block_order: int32 [4, 8], P('segment'), may hold values from 0 to 7, each once within a row
Outputs:
- layer_out: bfloat16 [4, 512, 2304], P('segment', 'tok')
- latent_act: bfloat16 [4, 512, 65536], P('segment', None, ('latent', 'tok'))
- recon: bfloat16 [4, 512, 2304], P('segment', 'tok')
- rates: float32 [4, 65536], P('segment', ('latent', 'tok'))
The draws below stay inside these ranges and needn't reach their ends.
All inputs are finite; a program needn't handle non-finite values.
Results may differ from the reference program's by a relative error of at most 0.014.
Values may be sent and summed in bfloat16 or wider, within the bound.
No kernel may reach another device: no remote copies, remote signals or barrier semaphores. Data moves between devices by JAX's collectives and lax.ppermute only.
A program may use at most 128 MiB of HBM per device.

```python
import jax
import jax.numpy as jnp
from jax import lax

D = 2304
LATENTS = 65536
BLOCKS = 8
SECTIONS = 4
ROWS = 512
BLOCK_ROWS = 64


def draw_window(key, part):
    first_key, second_key = jax.random.split(key)
    base = jax.random.normal(first_key, (ROWS, D), jnp.float32)
    offsets = 1.5 * jax.random.normal(second_key, (BLOCKS, D), jnp.float32)
    spread_rows = jnp.repeat(offsets, BLOCK_ROWS, axis=0)
    return jnp.clip(base + spread_rows, -8.0, 8.0).astype(jnp.bfloat16)


def plant(array, stream_key, least, top_value):
    longest = array.shape.index(max(array.shape))
    spots = []
    for shift in (0, 1):
        where = [jax.random.randint(jax.random.fold_in(stream_key, axis), (), 0, length) for axis, length in enumerate(array.shape)]
        where[longest] = (where[longest] + shift) % array.shape[longest]
        spots.append(tuple(where))
    return array.at[spots[0]].set(least).at[spots[1]].set(top_value)


def levels(rng, extent, pieces, low, top_value):
    loudness = 1.0
    for dim, shards_of in pieces:
        steps = jax.random.uniform(jax.random.fold_in(jax.random.fold_in(rng, 6), dim), (shards_of,), jnp.float32, low / len(pieces), top_value / len(pieces))
        loudness = loudness * jnp.repeat(jnp.exp(steps), extent[dim] // shards_of).reshape((-1,) + (1,) * (len(extent) - 1 - dim))
    return loudness


def noise(rng, extent, scale, bound, cuts=(), kind=jnp.bfloat16):
    result = jax.random.normal(rng, extent, jnp.float32) * scale
    if len(cuts) > 0:
        result = levels(rng, extent, cuts, -0.22, 0.18) * result
    return jnp.clip(result, min=-bound, max=bound).astype(kind)


def setup_inputs(seed: int = 0) -> dict:
    splits = jax.random.split(jax.random.key(seed), 10)
    return {
        "window": draw_window(jax.random.fold_in(splits[9], 71), 0),
        "norm_gain": jnp.clip(1.0 + 0.15 * jax.random.normal(splits[1], (SECTIONS, D), jnp.float32), 0.25, 1.75),
        "enc_weight": noise(splits[2], (SECTIONS, D, LATENTS), D ** -0.5, 0.125, ((0, 4), (2, 32))),
        "enc_bias": noise(splits[3], (SECTIONS, LATENTS), 0.3, 1.5, ((0, 4), (1, 32)), jnp.float32),
        "thresholds": plant(jax.random.randint(splits[4], (SECTIONS, LATENTS), 256, 1536), jax.random.fold_in(splits[4], 1), 256, 1535).astype(jnp.int32),
        "dec_weight": noise(splits[5], (SECTIONS, LATENTS, D), (LATENTS // 4) ** -0.5, 0.046875, ((0, 4), (1, 32))),
        "dec_bias": noise(splits[6], (SECTIONS, D), 0.5, 2.5, ((0, 4),), jnp.float32),
        "rates_start": jnp.clip(1.0 * jax.random.uniform(splits[7], (SECTIONS, LATENTS), jnp.float32) ** levels(splits[7], (SECTIONS, LATENTS), ((0, 4), (1, 32)), -0.2, 0.2), 0.0, 1.0),
        "block_order": jax.vmap(lambda own: jax.random.permutation(own, BLOCKS))(jax.random.split(splits[8], SECTIONS)).reshape((SECTIONS, BLOCKS)).astype(jnp.int32),
    }


EPSILON = 1e-06
SHARPNESS = 20.0
RATE_DECAY = 0.8

def reference(window, norm_gain, enc_weight, enc_bias, thresholds, dec_weight, dec_bias, rates_start, block_order):
    stream = window
    layer_list, latent_list, recon_list, rate_list = ([], [], [], [])
    for section in range(SECTIONS):
        hidden = stream.astype(jnp.float32)
        scale = lax.rsqrt(lax.optimization_barrier(jnp.mean(hidden * hidden, axis=-1, keepdims=True)) + EPSILON)
        normed = (hidden * scale * norm_gain[section][None, :]).astype(jnp.bfloat16)
        pre_act = jnp.dot(normed, enc_weight[section], preferred_element_type=jnp.float32) + enc_bias[section][None, :]
        theta = thresholds[section].astype(jnp.float32) / 1024.0
        fire_gate = jax.nn.sigmoid(SHARPNESS * (pre_act - theta[None, :]))
        latents = (pre_act * fire_gate).astype(jnp.bfloat16)
        recon_sum = jnp.dot(latents, dec_weight[section], preferred_element_type=jnp.float32) + dec_bias[section][None, :]
        layer = (hidden + recon_sum).astype(jnp.bfloat16)
        block_rate = lax.optimization_barrier(jnp.mean(fire_gate.reshape(BLOCKS, BLOCK_ROWS, LATENTS), axis=1))
        onehot = (block_order[section][:, None] == jnp.arange(BLOCKS, dtype=jnp.int32)[None, :]).astype(jnp.float32)
        position = jnp.dot(jnp.arange(BLOCKS).astype(jnp.float32), onehot, precision=lax.Precision.HIGHEST)
        weights = (1.0 - RATE_DECAY) * jnp.power(jnp.float32(RATE_DECAY), BLOCKS - 1.0 - position)
        final = RATE_DECAY ** BLOCKS * rates_start[section] + jnp.dot(weights, block_rate, precision=lax.Precision.HIGHEST)
        layer_list.append(layer)
        latent_list.append(latents)
        recon_list.append(recon_sum.astype(jnp.bfloat16))
        rate_list.append(final)
        stream = layer
    return (jnp.stack(layer_list), jnp.stack(latent_list), jnp.stack(recon_list), jnp.stack(rate_list))
```

```python
import jax
import jax.numpy as jnp
from jax import lax
from jax.sharding import PartitionSpec as P

ROWS_DEV = 128
MICRO = 8
BLOCKS = 8


EPSILON = 1e-06
SHARPNESS = 20.0
RATE_DECAY = 0.8


def from_behind(array, axis, by):
    devices = lax.axis_size(axis)
    pairs = [(i, i + by) for i in range(devices) if 0 <= i + by < devices]
    return lax.ppermute(array, axis, pairs)


def swap_with(array, axis, bit):
    devices = lax.axis_size(axis)
    return lax.ppermute(array, axis, [(i, i ^ bit) for i in range(devices)])


def reduce_rows(partial_sum, local_rows):
    width = partial_sum.shape[1]
    tok_index = lax.axis_index("tok")
    core = tok_index % 2
    low = tok_index // 2
    blocks = partial_sum.reshape(2, 2, local_rows, width)
    keep = lax.dynamic_index_in_dim(blocks, core, axis=1, keepdims=False)
    send = lax.dynamic_index_in_dim(blocks, 1 - core, axis=1, keepdims=False)
    halves = keep + swap_with(send, "tok", 1)
    keep = lax.dynamic_index_in_dim(halves, low, axis=0, keepdims=False)
    send = lax.dynamic_index_in_dim(halves, 1 - low, axis=0, keepdims=False)
    total = keep + swap_with(send, "tok", 2)
    for bit in (4, 1, 2):
        total = total + swap_with(total, "latent", bit)
    return total


def per_device(
    window,
    norm_gain,
    enc_weight,
    enc_bias,
    thresholds,
    dec_weight,
    dec_bias,
    rates_start,
    block_order,
):
    tok_count = lax.axis_size("tok")
    my_index = lax.axis_index("tok")
    segment_count = lax.axis_size("segment")
    segment_index = lax.axis_index("segment")
    local_rows = ROWS_DEV // MICRO
    width = window.shape[1]
    encoder = enc_weight[0]
    decoder = dec_weight[0]
    lat_local = encoder.shape[1]
    gain_row = norm_gain[0][None, :]
    enc_row = enc_bias[0][None, :]
    theta_row = thresholds[0].astype(jnp.float32)[None, :] / 1024.0
    dec_row = dec_bias[0][None, :]
    all_rows = ROWS_DEV * tok_count
    block_rows = all_rows // BLOCKS
    onehot = (block_order[0][:, None] == jnp.arange(BLOCKS, dtype=jnp.int32)[None, :]).astype(
        jnp.float32
    )
    position = jnp.dot(
        jnp.arange(BLOCKS).astype(jnp.float32), onehot, precision=lax.Precision.HIGHEST
    )
    block_weight = (1.0 - RATE_DECAY) * jnp.power(jnp.float32(RATE_DECAY), BLOCKS - 1.0 - position)
    row_weight = jnp.repeat(block_weight / block_rows, block_rows).reshape(
        tok_count, MICRO, local_rows
    )
    carried = jnp.zeros((local_rows, width), jnp.bfloat16)
    layer_buf = jnp.zeros((ROWS_DEV, width), jnp.bfloat16)
    recon_buf = jnp.zeros((ROWS_DEV, width), jnp.bfloat16)
    latent_buf = jnp.zeros((tok_count, MICRO, local_rows, lat_local), jnp.bfloat16)
    rate_acc = jnp.zeros((lat_local,), jnp.float32)
    for tick in range(MICRO + segment_count - 1):
        micro_here = tick - segment_index
        valid = jnp.logical_and(micro_here >= 0, micro_here < MICRO)
        micro_idx = jnp.clip(micro_here, 0, MICRO - 1)
        if tick < MICRO:
            fresh = window[tick * local_rows : (tick + 1) * local_rows]
        else:
            fresh = jnp.zeros((local_rows, width), jnp.bfloat16)
        incoming = jnp.where(segment_index == 0, fresh, carried)
        hidden = incoming.astype(jnp.float32)
        scale = lax.rsqrt(jnp.mean(hidden * hidden, axis=-1, keepdims=True) + EPSILON)
        normed = (hidden * scale * gain_row).astype(jnp.bfloat16)
        pre_act = (
            jnp.dot(
                lax.all_gather(normed, "tok", axis=0, tiled=True),
                encoder,
                preferred_element_type=jnp.float32,
            )
            + enc_row
        )
        fire_gate = jax.nn.sigmoid(SHARPNESS * (pre_act - theta_row))
        latents = (pre_act * fire_gate).astype(jnp.bfloat16)
        weights_now = lax.dynamic_slice(
            row_weight, (0, micro_idx, 0), (tok_count, 1, local_rows)
        ).reshape(-1)
        rate_term = jnp.dot(weights_now, fire_gate, precision=lax.Precision.HIGHEST)
        rate_acc = rate_acc + jnp.where(valid, rate_term, 0.0)
        latent_grid = latents.reshape(tok_count, 1, local_rows, lat_local)
        previous = lax.dynamic_slice(
            latent_buf, (0, micro_idx, 0, 0), (tok_count, 1, local_rows, lat_local)
        )
        latent_buf = lax.dynamic_update_slice(
            latent_buf, jnp.where(valid, latent_grid, previous), (0, micro_idx, 0, 0)
        )
        partial_sum = jnp.dot(latents, decoder, preferred_element_type=jnp.float32)
        mine = reduce_rows(partial_sum, local_rows)
        recon_sum = mine + dec_row
        layer = (hidden + recon_sum).astype(jnp.bfloat16)
        recon_now = recon_sum.astype(jnp.bfloat16)
        row_start = micro_idx * local_rows
        old_layer = lax.dynamic_slice_in_dim(layer_buf, row_start, local_rows, 0)
        layer_buf = lax.dynamic_update_slice_in_dim(
            layer_buf, jnp.where(valid, layer, old_layer), row_start, 0
        )
        old_recon = lax.dynamic_slice_in_dim(recon_buf, row_start, local_rows, 0)
        recon_buf = lax.dynamic_update_slice_in_dim(
            recon_buf, jnp.where(valid, recon_now, old_recon), row_start, 0
        )
        carried = from_behind(layer, "segment", 1)
    final_rates = RATE_DECAY**BLOCKS * rates_start[0] + rate_acc
    latent_out = latent_buf.reshape(tok_count * ROWS_DEV, lat_local)
    return (layer_buf[None], latent_out[None], recon_buf[None], final_rates[None])


def solution(mesh):
    placed = (
        P("tok", None),
        P("segment", None),
        P("segment", None, ("latent", "tok")),
        P("segment", ("latent", "tok")),
        P("segment", ("latent", "tok")),
        P("segment", ("latent", "tok"), None),
        P("segment", None),
        P("segment", ("latent", "tok")),
        P("segment", None),
    )
    return jax.shard_map(
        per_device,
        mesh=mesh,
        in_specs=placed,
        out_specs=(
            P("segment", "tok", None),
            P("segment", None, ("latent", "tok")),
            P("segment", "tok", None),
            P("segment", ("latent", "tok")),
        ),
        check_vma=False,
    )
```

```python
import jax
import jax.numpy as jnp
from jax import lax
from jax.sharding import PartitionSpec as P

ROWS_DEV = 128
MICRO = 4
BLOCKS = 8


EPSILON = 1e-06
SHARPNESS = 20.0
RATE_DECAY = 0.8


def from_behind(array, axis, by):
    devices = lax.axis_size(axis)
    pairs = [(i, i + by) for i in range(devices) if 0 <= i + by < devices]
    return lax.ppermute(array, axis, pairs)


def swap_with(array, axis, bit):
    devices = lax.axis_size(axis)
    return lax.ppermute(array, axis, [(i, i ^ bit) for i in range(devices)])


def reduce_rows(partial_sum, local_rows):
    width = partial_sum.shape[1]
    tok_index = lax.axis_index("tok")
    core = tok_index % 2
    low = tok_index // 2
    blocks = partial_sum.reshape(2, 2, local_rows, width)
    keep = lax.dynamic_index_in_dim(blocks, core, axis=1, keepdims=False)
    send = lax.dynamic_index_in_dim(blocks, 1 - core, axis=1, keepdims=False)
    halves = keep + swap_with(send, "tok", 1)
    keep = lax.dynamic_index_in_dim(halves, low, axis=0, keepdims=False)
    send = lax.dynamic_index_in_dim(halves, 1 - low, axis=0, keepdims=False)
    total = keep + swap_with(send, "tok", 2)
    for step in range(3):
        total = total + lax.ppermute(total, ("latent", "tok"), latent_round(step))
    return total


def latent_round(step):
    orders = ((4, 1, 2), (2, 4, 1))
    pairs = []
    for latent in range(8):
        for tok in range(4):
            bit = orders[tok % 2][step]
            pairs.append((latent * 4 + tok, (latent ^ bit) * 4 + tok))
    return pairs


def per_device(
    window,
    norm_gain,
    enc_weight,
    enc_bias,
    thresholds,
    dec_weight,
    dec_bias,
    rates_start,
    block_order,
):
    tok_count = lax.axis_size("tok")
    my_index = lax.axis_index("tok")
    segment_count = lax.axis_size("segment")
    segment_index = lax.axis_index("segment")
    local_rows = ROWS_DEV // MICRO
    width = window.shape[1]
    encoder = enc_weight[0]
    decoder = dec_weight[0]
    lat_local = encoder.shape[1]
    gain_row = norm_gain[0][None, :]
    enc_row = enc_bias[0][None, :]
    theta_row = thresholds[0].astype(jnp.float32)[None, :] / 1024.0
    dec_row = dec_bias[0][None, :]
    all_rows = ROWS_DEV * tok_count
    block_rows = all_rows // BLOCKS
    onehot = (block_order[0][:, None] == jnp.arange(BLOCKS, dtype=jnp.int32)[None, :]).astype(
        jnp.float32
    )
    position = jnp.dot(
        jnp.arange(BLOCKS).astype(jnp.float32), onehot, precision=lax.Precision.HIGHEST
    )
    block_weight = (1.0 - RATE_DECAY) * jnp.power(jnp.float32(RATE_DECAY), BLOCKS - 1.0 - position)
    row_weight = jnp.repeat(block_weight / block_rows, block_rows).reshape(
        tok_count, MICRO, local_rows
    )
    carried = jnp.zeros((local_rows, width), jnp.bfloat16)
    layer_buf = jnp.zeros((ROWS_DEV, width), jnp.bfloat16)
    recon_buf = jnp.zeros((ROWS_DEV, width), jnp.bfloat16)
    latent_buf = jnp.zeros((tok_count, MICRO, local_rows, lat_local), jnp.bfloat16)
    rate_acc = jnp.zeros((lat_local,), jnp.float32)
    for tick in range(MICRO + segment_count - 1):
        micro_here = tick - segment_index
        valid = jnp.logical_and(micro_here >= 0, micro_here < MICRO)
        micro_idx = jnp.clip(micro_here, 0, MICRO - 1)
        if tick < MICRO:
            fresh = window[tick * local_rows : (tick + 1) * local_rows]
        else:
            fresh = jnp.zeros((local_rows, width), jnp.bfloat16)
        incoming = jnp.where(segment_index == 0, fresh, carried)
        hidden = incoming.astype(jnp.float32)
        scale = lax.rsqrt(jnp.mean(hidden * hidden, axis=-1, keepdims=True) + EPSILON)
        normed = (hidden * scale * gain_row).astype(jnp.bfloat16)
        pre_act = (
            jnp.dot(
                lax.all_gather(normed, "tok", axis=0, tiled=True),
                encoder,
                preferred_element_type=jnp.float32,
            )
            + enc_row
        )
        fire_gate = jax.nn.sigmoid(SHARPNESS * (pre_act - theta_row))
        latents = (pre_act * fire_gate).astype(jnp.bfloat16)
        weights_now = lax.dynamic_slice(
            row_weight, (0, micro_idx, 0), (tok_count, 1, local_rows)
        ).reshape(-1)
        rate_term = jnp.dot(weights_now, fire_gate, precision=lax.Precision.HIGHEST)
        rate_acc = rate_acc + jnp.where(valid, rate_term, 0.0)
        latent_grid = latents.reshape(tok_count, 1, local_rows, lat_local)
        previous = lax.dynamic_slice(
            latent_buf, (0, micro_idx, 0, 0), (tok_count, 1, local_rows, lat_local)
        )
        latent_buf = lax.dynamic_update_slice(
            latent_buf, jnp.where(valid, latent_grid, previous), (0, micro_idx, 0, 0)
        )
        partial_sum = jnp.dot(latents, decoder, preferred_element_type=jnp.float32)
        mine = reduce_rows(partial_sum, local_rows)
        recon_sum = mine + dec_row
        layer = (hidden + recon_sum).astype(jnp.bfloat16)
        recon_now = recon_sum.astype(jnp.bfloat16)
        row_start = micro_idx * local_rows
        old_layer = lax.dynamic_slice_in_dim(layer_buf, row_start, local_rows, 0)
        layer_buf = lax.dynamic_update_slice_in_dim(
            layer_buf, jnp.where(valid, layer, old_layer), row_start, 0
        )
        old_recon = lax.dynamic_slice_in_dim(recon_buf, row_start, local_rows, 0)
        recon_buf = lax.dynamic_update_slice_in_dim(
            recon_buf, jnp.where(valid, recon_now, old_recon), row_start, 0
        )
        carried = from_behind(layer, "segment", 1)
    final_rates = RATE_DECAY**BLOCKS * rates_start[0] + rate_acc
    latent_out = latent_buf.reshape(tok_count * ROWS_DEV, lat_local)
    return (layer_buf[None], latent_out[None], recon_buf[None], final_rates[None])


def solution(mesh):
    placed = (
        P("tok", None),
        P("segment", None),
        P("segment", None, ("latent", "tok")),
        P("segment", ("latent", "tok")),
        P("segment", ("latent", "tok")),
        P("segment", ("latent", "tok"), None),
        P("segment", None),
        P("segment", ("latent", "tok")),
        P("segment", None),
    )
    return jax.shard_map(
        per_device,
        mesh=mesh,
        in_specs=placed,
        out_specs=(
            P("segment", "tok", None),
            P("segment", None, ("latent", "tok")),
            P("segment", "tok", None),
            P("segment", ("latent", "tok")),
        ),
        check_vma=False,
    )
```

```python
import jax
import jax.numpy as jnp
from jax import lax
from jax.sharding import PartitionSpec as P

ROWS_DEV = 128
MICRO = 4
BLOCKS = 8


EPSILON = 1e-06
SHARPNESS = 20.0
RATE_DECAY = 0.8


def from_behind(array, axis, by):
    devices = lax.axis_size(axis)
    pairs = [(i, i + by) for i in range(devices) if 0 <= i + by < devices]
    return lax.ppermute(array, axis, pairs)


def swap_with(array, axis, bit):
    devices = lax.axis_size(axis)
    return lax.ppermute(array, axis, [(i, i ^ bit) for i in range(devices)])


def reduce_rows(partial_sum, local_rows):
    width = partial_sum.shape[1]
    tok_index = lax.axis_index("tok")
    core = tok_index % 2
    low = tok_index // 2
    blocks = partial_sum.reshape(2, 2, local_rows, width)
    keep = lax.dynamic_index_in_dim(blocks, core, axis=1, keepdims=False)
    send = lax.dynamic_index_in_dim(blocks, 1 - core, axis=1, keepdims=False)
    halves = keep + widen(swap_with(send.astype(jnp.bfloat16), "tok", 1))
    keep = lax.dynamic_index_in_dim(halves, low, axis=0, keepdims=False)
    send = lax.dynamic_index_in_dim(halves, 1 - low, axis=0, keepdims=False)
    total = keep + widen(swap_with(send.astype(jnp.bfloat16), "tok", 2))
    for step in range(3):
        narrow = total.astype(jnp.bfloat16)
        total = widen(narrow) + widen(
            lax.ppermute(narrow, ("latent", "tok"), latent_round(step))
        )
    return total


def widen(array):
    return array.astype(jnp.float32)


def latent_round(step):
    orders = ((4, 1, 2), (2, 4, 1))
    pairs = []
    for latent in range(8):
        for tok in range(4):
            bit = orders[tok % 2][step]
            pairs.append((latent * 4 + tok, (latent ^ bit) * 4 + tok))
    return pairs


def per_device(
    window,
    norm_gain,
    enc_weight,
    enc_bias,
    thresholds,
    dec_weight,
    dec_bias,
    rates_start,
    block_order,
):
    tok_count = lax.axis_size("tok")
    my_index = lax.axis_index("tok")
    segment_count = lax.axis_size("segment")
    segment_index = lax.axis_index("segment")
    local_rows = ROWS_DEV // MICRO
    width = window.shape[1]
    encoder = enc_weight[0]
    decoder = dec_weight[0]
    lat_local = encoder.shape[1]
    gain_row = norm_gain[0][None, :]
    enc_row = enc_bias[0][None, :]
    theta_row = thresholds[0].astype(jnp.float32)[None, :] / 1024.0
    dec_row = dec_bias[0][None, :]
    all_rows = ROWS_DEV * tok_count
    block_rows = all_rows // BLOCKS
    onehot = (block_order[0][:, None] == jnp.arange(BLOCKS, dtype=jnp.int32)[None, :]).astype(
        jnp.float32
    )
    position = jnp.dot(
        jnp.arange(BLOCKS).astype(jnp.float32), onehot, precision=lax.Precision.HIGHEST
    )
    block_weight = (1.0 - RATE_DECAY) * jnp.power(jnp.float32(RATE_DECAY), BLOCKS - 1.0 - position)
    row_weight = jnp.repeat(block_weight / block_rows, block_rows).reshape(
        tok_count, MICRO, local_rows
    )
    carried = jnp.zeros((local_rows, width), jnp.bfloat16)
    layer_buf = jnp.zeros((ROWS_DEV, width), jnp.bfloat16)
    recon_buf = jnp.zeros((ROWS_DEV, width), jnp.bfloat16)
    latent_buf = jnp.zeros((tok_count, MICRO, local_rows, lat_local), jnp.bfloat16)
    rate_acc = jnp.zeros((lat_local,), jnp.float32)
    for tick in range(MICRO + segment_count - 1):
        micro_here = tick - segment_index
        valid = jnp.logical_and(micro_here >= 0, micro_here < MICRO)
        micro_idx = jnp.clip(micro_here, 0, MICRO - 1)
        if tick < MICRO:
            fresh = window[tick * local_rows : (tick + 1) * local_rows]
        else:
            fresh = jnp.zeros((local_rows, width), jnp.bfloat16)
        incoming = jnp.where(segment_index == 0, fresh, carried)
        hidden = incoming.astype(jnp.float32)
        scale = lax.rsqrt(jnp.mean(hidden * hidden, axis=-1, keepdims=True) + EPSILON)
        normed = (hidden * scale * gain_row).astype(jnp.bfloat16)
        pre_act = (
            jnp.dot(
                lax.all_gather(normed, "tok", axis=0, tiled=True),
                encoder,
                preferred_element_type=jnp.float32,
            )
            + enc_row
        )
        fire_gate = jax.nn.sigmoid(SHARPNESS * (pre_act - theta_row))
        latents = (pre_act * fire_gate).astype(jnp.bfloat16)
        weights_now = lax.dynamic_slice(
            row_weight, (0, micro_idx, 0), (tok_count, 1, local_rows)
        ).reshape(-1)
        rate_term = jnp.dot(weights_now, fire_gate, precision=lax.Precision.HIGHEST)
        rate_acc = rate_acc + jnp.where(valid, rate_term, 0.0)
        latent_grid = latents.reshape(tok_count, 1, local_rows, lat_local)
        previous = lax.dynamic_slice(
            latent_buf, (0, micro_idx, 0, 0), (tok_count, 1, local_rows, lat_local)
        )
        latent_buf = lax.dynamic_update_slice(
            latent_buf, jnp.where(valid, latent_grid, previous), (0, micro_idx, 0, 0)
        )
        partial_sum = jnp.dot(latents, decoder, preferred_element_type=jnp.float32)
        mine = reduce_rows(partial_sum, local_rows)
        recon_sum = mine + dec_row
        layer = (hidden + recon_sum).astype(jnp.bfloat16)
        recon_now = recon_sum.astype(jnp.bfloat16)
        row_start = micro_idx * local_rows
        old_layer = lax.dynamic_slice_in_dim(layer_buf, row_start, local_rows, 0)
        layer_buf = lax.dynamic_update_slice_in_dim(
            layer_buf, jnp.where(valid, layer, old_layer), row_start, 0
        )
        old_recon = lax.dynamic_slice_in_dim(recon_buf, row_start, local_rows, 0)
        recon_buf = lax.dynamic_update_slice_in_dim(
            recon_buf, jnp.where(valid, recon_now, old_recon), row_start, 0
        )
        carried = from_behind(layer, "segment", 1)
    final_rates = RATE_DECAY**BLOCKS * rates_start[0] + rate_acc
    latent_out = latent_buf.reshape(tok_count * ROWS_DEV, lat_local)
    return (layer_buf[None], latent_out[None], recon_buf[None], final_rates[None])


def solution(mesh):
    placed = (
        P("tok", None),
        P("segment", None),
        P("segment", None, ("latent", "tok")),
        P("segment", ("latent", "tok")),
        P("segment", ("latent", "tok")),
        P("segment", ("latent", "tok"), None),
        P("segment", None),
        P("segment", ("latent", "tok")),
        P("segment", None),
    )
    return jax.shard_map(
        per_device,
        mesh=mesh,
        in_specs=placed,
        out_specs=(
            P("segment", "tok", None),
            P("segment", None, ("latent", "tok")),
            P("segment", "tok", None),
            P("segment", ("latent", "tok")),
        ),
        check_vma=False,
    )
```

```python
import jax
import jax.numpy as jnp
from jax import lax
from jax.sharding import PartitionSpec as P

ROWS_DEV = 128
MICRO = 4
BLOCKS = 8


EPSILON = 1e-06
SHARPNESS = 20.0
RATE_DECAY = 0.8


def from_behind(array, axis, by):
    devices = lax.axis_size(axis)
    pairs = [(i, i + by) for i in range(devices) if 0 <= i + by < devices]
    return lax.ppermute(array, axis, pairs)


def swap_with(array, axis, bit):
    devices = lax.axis_size(axis)
    return lax.ppermute(array, axis, [(i, i ^ bit) for i in range(devices)])


def reduce_rows(partial_sum, local_rows):
    width = partial_sum.shape[1]
    tok_index = lax.axis_index("tok")
    core = tok_index % 2
    low = tok_index // 2
    blocks = partial_sum.reshape(2, 2, local_rows, width)
    keep = lax.dynamic_index_in_dim(blocks, core, axis=1, keepdims=False)
    send = lax.dynamic_index_in_dim(blocks, 1 - core, axis=1, keepdims=False)
    halves = keep + widen(swap_with(send.astype(jnp.bfloat16), "tok", 1))
    keep = lax.dynamic_index_in_dim(halves, low, axis=0, keepdims=False)
    send = lax.dynamic_index_in_dim(halves, 1 - low, axis=0, keepdims=False)
    total = keep + widen(swap_with(send.astype(jnp.bfloat16), "tok", 2))
    return spread_over_latent(total)


def spread_over_latent(total):
    count = lax.axis_size("latent")
    me = lax.axis_index("latent")
    pieces = total.reshape(count, total.shape[0] // count, total.shape[1])
    piece = lax.dynamic_index_in_dim(pieces, me, axis=0, keepdims=False)
    for bit in range(1, count):
        send = lax.dynamic_index_in_dim(pieces, me ^ bit, axis=0, keepdims=False)
        piece = piece + widen(swap_with(send.astype(jnp.bfloat16), "latent", bit))
    gathered = [None] * count
    gathered[0] = piece
    for bit in range(1, count):
        gathered[bit] = swap_with(piece, "latent", bit)
    stacked = jnp.stack(gathered)
    order = jnp.arange(count) ^ me
    return jnp.take(stacked, order, axis=0).reshape(total.shape)


def widen(array):
    return array.astype(jnp.float32)


def latent_round(step):
    orders = ((4, 1, 2), (2, 4, 1))
    pairs = []
    for latent in range(8):
        for tok in range(4):
            bit = orders[tok % 2][step]
            pairs.append((latent * 4 + tok, (latent ^ bit) * 4 + tok))
    return pairs


def per_device(
    window,
    norm_gain,
    enc_weight,
    enc_bias,
    thresholds,
    dec_weight,
    dec_bias,
    rates_start,
    block_order,
):
    tok_count = lax.axis_size("tok")
    my_index = lax.axis_index("tok")
    segment_count = lax.axis_size("segment")
    segment_index = lax.axis_index("segment")
    local_rows = ROWS_DEV // MICRO
    width = window.shape[1]
    encoder = enc_weight[0]
    decoder = dec_weight[0]
    lat_local = encoder.shape[1]
    gain_row = norm_gain[0][None, :]
    enc_row = enc_bias[0][None, :]
    theta_row = thresholds[0].astype(jnp.float32)[None, :] / 1024.0
    dec_row = dec_bias[0][None, :]
    all_rows = ROWS_DEV * tok_count
    block_rows = all_rows // BLOCKS
    onehot = (block_order[0][:, None] == jnp.arange(BLOCKS, dtype=jnp.int32)[None, :]).astype(
        jnp.float32
    )
    position = jnp.dot(
        jnp.arange(BLOCKS).astype(jnp.float32), onehot, precision=lax.Precision.HIGHEST
    )
    block_weight = (1.0 - RATE_DECAY) * jnp.power(jnp.float32(RATE_DECAY), BLOCKS - 1.0 - position)
    row_weight = jnp.repeat(block_weight / block_rows, block_rows).reshape(
        tok_count, MICRO, local_rows
    )
    carried = jnp.zeros((local_rows, width), jnp.bfloat16)
    layer_buf = jnp.zeros((ROWS_DEV, width), jnp.bfloat16)
    recon_buf = jnp.zeros((ROWS_DEV, width), jnp.bfloat16)
    latent_buf = jnp.zeros((tok_count, MICRO, local_rows, lat_local), jnp.bfloat16)
    rate_acc = jnp.zeros((lat_local,), jnp.float32)
    for tick in range(MICRO + segment_count - 1):
        micro_here = tick - segment_index
        valid = jnp.logical_and(micro_here >= 0, micro_here < MICRO)
        micro_idx = jnp.clip(micro_here, 0, MICRO - 1)
        if tick < MICRO:
            fresh = window[tick * local_rows : (tick + 1) * local_rows]
        else:
            fresh = jnp.zeros((local_rows, width), jnp.bfloat16)
        incoming = jnp.where(segment_index == 0, fresh, carried)
        hidden = incoming.astype(jnp.float32)
        scale = lax.rsqrt(jnp.mean(hidden * hidden, axis=-1, keepdims=True) + EPSILON)
        normed = (hidden * scale * gain_row).astype(jnp.bfloat16)
        pre_act = (
            jnp.dot(
                lax.all_gather(normed, "tok", axis=0, tiled=True),
                encoder,
                preferred_element_type=jnp.float32,
            )
            + enc_row
        )
        fire_gate = jax.nn.sigmoid(SHARPNESS * (pre_act - theta_row))
        latents = (pre_act * fire_gate).astype(jnp.bfloat16)
        weights_now = lax.dynamic_slice(
            row_weight, (0, micro_idx, 0), (tok_count, 1, local_rows)
        ).reshape(-1)
        rate_term = jnp.dot(weights_now, fire_gate, precision=lax.Precision.HIGHEST)
        rate_acc = rate_acc + jnp.where(valid, rate_term, 0.0)
        latent_grid = latents.reshape(tok_count, 1, local_rows, lat_local)
        previous = lax.dynamic_slice(
            latent_buf, (0, micro_idx, 0, 0), (tok_count, 1, local_rows, lat_local)
        )
        latent_buf = lax.dynamic_update_slice(
            latent_buf, jnp.where(valid, latent_grid, previous), (0, micro_idx, 0, 0)
        )
        partial_sum = jnp.dot(latents, decoder, preferred_element_type=jnp.float32)
        mine = reduce_rows(partial_sum, local_rows)
        recon_sum = mine + dec_row
        layer = (hidden + recon_sum).astype(jnp.bfloat16)
        recon_now = recon_sum.astype(jnp.bfloat16)
        row_start = micro_idx * local_rows
        old_layer = lax.dynamic_slice_in_dim(layer_buf, row_start, local_rows, 0)
        layer_buf = lax.dynamic_update_slice_in_dim(
            layer_buf, jnp.where(valid, layer, old_layer), row_start, 0
        )
        old_recon = lax.dynamic_slice_in_dim(recon_buf, row_start, local_rows, 0)
        recon_buf = lax.dynamic_update_slice_in_dim(
            recon_buf, jnp.where(valid, recon_now, old_recon), row_start, 0
        )
        carried = from_behind(layer, "segment", 1)
    final_rates = RATE_DECAY**BLOCKS * rates_start[0] + rate_acc
    latent_out = latent_buf.reshape(tok_count * ROWS_DEV, lat_local)
    return (layer_buf[None], latent_out[None], recon_buf[None], final_rates[None])


def solution(mesh):
    placed = (
        P("tok", None),
        P("segment", None),
        P("segment", None, ("latent", "tok")),
        P("segment", ("latent", "tok")),
        P("segment", ("latent", "tok")),
        P("segment", ("latent", "tok"), None),
        P("segment", None),
        P("segment", ("latent", "tok")),
        P("segment", None),
    )
    return jax.shard_map(
        per_device,
        mesh=mesh,
        in_specs=placed,
        out_specs=(
            P("segment", "tok", None),
            P("segment", None, ("latent", "tok")),
            P("segment", "tok", None),
            P("segment", ("latent", "tok")),
        ),
        check_vma=False,
    )
```

```python
import jax
import jax.numpy as jnp
from jax import lax
from jax.sharding import PartitionSpec as P

ROWS_DEV = 128
MICRO = 2
BLOCKS = 8


EPSILON = 1e-06
SHARPNESS = 20.0
RATE_DECAY = 0.8


def from_behind(array, axis, by):
    devices = lax.axis_size(axis)
    pairs = [(i, i + by) for i in range(devices) if 0 <= i + by < devices]
    return lax.ppermute(array, axis, pairs)


def swap_with(array, axis, bit):
    devices = lax.axis_size(axis)
    return lax.ppermute(array, axis, [(i, i ^ bit) for i in range(devices)])


def reduce_rows(partial_sum, local_rows):
    width = partial_sum.shape[1]
    tok_index = lax.axis_index("tok")
    core = tok_index % 2
    low = tok_index // 2
    blocks = partial_sum.reshape(2, 2, local_rows, width)
    keep = lax.dynamic_index_in_dim(blocks, core, axis=1, keepdims=False)
    send = lax.dynamic_index_in_dim(blocks, 1 - core, axis=1, keepdims=False)
    halves = keep + widen(swap_with(send.astype(jnp.bfloat16), "tok", 1))
    keep = lax.dynamic_index_in_dim(halves, low, axis=0, keepdims=False)
    send = lax.dynamic_index_in_dim(halves, 1 - low, axis=0, keepdims=False)
    total = keep + widen(swap_with(send.astype(jnp.bfloat16), "tok", 2))
    for step in range(3):
        narrow = total.astype(jnp.bfloat16)
        total = widen(narrow) + widen(
            lax.ppermute(narrow, ("latent", "tok"), latent_round(step))
        )
    return total


def widen(array):
    return array.astype(jnp.float32)


def latent_round(step):
    orders = ((4, 1, 2), (2, 4, 1))
    pairs = []
    for latent in range(8):
        for tok in range(4):
            bit = orders[tok % 2][step]
            pairs.append((latent * 4 + tok, (latent ^ bit) * 4 + tok))
    return pairs


def per_device(
    window,
    norm_gain,
    enc_weight,
    enc_bias,
    thresholds,
    dec_weight,
    dec_bias,
    rates_start,
    block_order,
):
    tok_count = lax.axis_size("tok")
    my_index = lax.axis_index("tok")
    segment_count = lax.axis_size("segment")
    segment_index = lax.axis_index("segment")
    local_rows = ROWS_DEV // MICRO
    width = window.shape[1]
    encoder = enc_weight[0]
    decoder = dec_weight[0]
    lat_local = encoder.shape[1]
    gain_row = norm_gain[0][None, :]
    enc_row = enc_bias[0][None, :]
    theta_row = thresholds[0].astype(jnp.float32)[None, :] / 1024.0
    dec_row = dec_bias[0][None, :]
    all_rows = ROWS_DEV * tok_count
    block_rows = all_rows // BLOCKS
    onehot = (block_order[0][:, None] == jnp.arange(BLOCKS, dtype=jnp.int32)[None, :]).astype(
        jnp.float32
    )
    position = jnp.dot(
        jnp.arange(BLOCKS).astype(jnp.float32), onehot, precision=lax.Precision.HIGHEST
    )
    block_weight = (1.0 - RATE_DECAY) * jnp.power(jnp.float32(RATE_DECAY), BLOCKS - 1.0 - position)
    row_weight = jnp.repeat(block_weight / block_rows, block_rows).reshape(
        tok_count, MICRO, local_rows
    )
    carried = jnp.zeros((local_rows, width), jnp.bfloat16)
    layer_buf = jnp.zeros((ROWS_DEV, width), jnp.bfloat16)
    recon_buf = jnp.zeros((ROWS_DEV, width), jnp.bfloat16)
    latent_buf = jnp.zeros((tok_count, MICRO, local_rows, lat_local), jnp.bfloat16)
    rate_acc = jnp.zeros((lat_local,), jnp.float32)
    for tick in range(MICRO + segment_count - 1):
        micro_here = tick - segment_index
        valid = jnp.logical_and(micro_here >= 0, micro_here < MICRO)
        micro_idx = jnp.clip(micro_here, 0, MICRO - 1)
        if tick < MICRO:
            fresh = window[tick * local_rows : (tick + 1) * local_rows]
        else:
            fresh = jnp.zeros((local_rows, width), jnp.bfloat16)
        incoming = jnp.where(segment_index == 0, fresh, carried)
        hidden = incoming.astype(jnp.float32)
        scale = lax.rsqrt(jnp.mean(hidden * hidden, axis=-1, keepdims=True) + EPSILON)
        normed = (hidden * scale * gain_row).astype(jnp.bfloat16)
        pre_act = (
            jnp.dot(
                lax.all_gather(normed, "tok", axis=0, tiled=True),
                encoder,
                preferred_element_type=jnp.float32,
            )
            + enc_row
        )
        fire_gate = jax.nn.sigmoid(SHARPNESS * (pre_act - theta_row))
        latents = (pre_act * fire_gate).astype(jnp.bfloat16)
        weights_now = lax.dynamic_slice(
            row_weight, (0, micro_idx, 0), (tok_count, 1, local_rows)
        ).reshape(-1)
        rate_term = jnp.dot(weights_now, fire_gate, precision=lax.Precision.HIGHEST)
        rate_acc = rate_acc + jnp.where(valid, rate_term, 0.0)
        latent_grid = latents.reshape(tok_count, 1, local_rows, lat_local)
        previous = lax.dynamic_slice(
            latent_buf, (0, micro_idx, 0, 0), (tok_count, 1, local_rows, lat_local)
        )
        latent_buf = lax.dynamic_update_slice(
            latent_buf, jnp.where(valid, latent_grid, previous), (0, micro_idx, 0, 0)
        )
        partial_sum = jnp.dot(latents, decoder, preferred_element_type=jnp.float32)
        mine = reduce_rows(partial_sum, local_rows)
        recon_sum = mine + dec_row
        layer = (hidden + recon_sum).astype(jnp.bfloat16)
        recon_now = recon_sum.astype(jnp.bfloat16)
        row_start = micro_idx * local_rows
        old_layer = lax.dynamic_slice_in_dim(layer_buf, row_start, local_rows, 0)
        layer_buf = lax.dynamic_update_slice_in_dim(
            layer_buf, jnp.where(valid, layer, old_layer), row_start, 0
        )
        old_recon = lax.dynamic_slice_in_dim(recon_buf, row_start, local_rows, 0)
        recon_buf = lax.dynamic_update_slice_in_dim(
            recon_buf, jnp.where(valid, recon_now, old_recon), row_start, 0
        )
        carried = from_behind(layer, "segment", 1)
    final_rates = RATE_DECAY**BLOCKS * rates_start[0] + rate_acc
    latent_out = latent_buf.reshape(tok_count * ROWS_DEV, lat_local)
    return (layer_buf[None], latent_out[None], recon_buf[None], final_rates[None])


def solution(mesh):
    placed = (
        P("tok", None),
        P("segment", None),
        P("segment", None, ("latent", "tok")),
        P("segment", ("latent", "tok")),
        P("segment", ("latent", "tok")),
        P("segment", ("latent", "tok"), None),
        P("segment", None),
        P("segment", ("latent", "tok")),
        P("segment", None),
    )
    return jax.shard_map(
        per_device,
        mesh=mesh,
        in_specs=placed,
        out_specs=(
            P("segment", "tok", None),
            P("segment", None, ("latent", "tok")),
            P("segment", "tok", None),
            P("segment", ("latent", "tok")),
        ),
        check_vma=False,
    )
```

```python
import jax
import jax.numpy as jnp
from jax import lax
from jax.sharding import PartitionSpec as P

ROWS_DEV = 128
MICRO = 4
BLOCKS = 8


EPSILON = 1e-06
SHARPNESS = 20.0
RATE_DECAY = 0.8


def from_behind(array, axis, by):
    devices = lax.axis_size(axis)
    pairs = [(i, i + by) for i in range(devices) if 0 <= i + by < devices]
    return lax.ppermute(array, axis, pairs)


def swap_with(array, axis, bit):
    devices = lax.axis_size(axis)
    return lax.ppermute(array, axis, [(i, i ^ bit) for i in range(devices)])


def reduce_rows(partial_sum, local_rows):
    width = partial_sum.shape[1]
    tok_index = lax.axis_index("tok")
    core = tok_index % 2
    low = tok_index // 2
    blocks = partial_sum.reshape(2, 2, local_rows, width)
    keep = lax.dynamic_index_in_dim(blocks, core, axis=1, keepdims=False)
    send = lax.dynamic_index_in_dim(blocks, 1 - core, axis=1, keepdims=False)
    halves = keep + widen(swap_with(send.astype(jnp.bfloat16), "tok", 1))
    keep = lax.dynamic_index_in_dim(halves, low, axis=0, keepdims=False)
    send = lax.dynamic_index_in_dim(halves, 1 - low, axis=0, keepdims=False)
    total = keep + widen(swap_with(send.astype(jnp.bfloat16), "tok", 2))
    for step in range(3):
        narrow = total.astype(jnp.bfloat16)
        total = widen(narrow) + widen(
            lax.ppermute(narrow, ("latent", "tok"), latent_round(step))
        )
    return total


def widen(array):
    return array.astype(jnp.float32)


def latent_round(step):
    orders = ((4, 1, 2), (2, 4, 1))
    pairs = []
    for latent in range(8):
        for tok in range(4):
            bit = orders[tok % 2][step]
            pairs.append((latent * 4 + tok, (latent ^ bit) * 4 + tok))
    return pairs


def per_device(
    window,
    norm_gain,
    enc_weight,
    enc_bias,
    thresholds,
    dec_weight,
    dec_bias,
    rates_start,
    block_order,
):
    tok_count = lax.axis_size("tok")
    my_index = lax.axis_index("tok")
    segment_count = lax.axis_size("segment")
    segment_index = lax.axis_index("segment")
    local_rows = ROWS_DEV // MICRO
    width = window.shape[1]
    encoder = enc_weight[0]
    decoder = dec_weight[0]
    lat_local = encoder.shape[1]
    gain_row = norm_gain[0][None, :]
    enc_row = enc_bias[0][None, :]
    theta_row = thresholds[0].astype(jnp.float32)[None, :] / 1024.0
    dec_row = dec_bias[0][None, :]
    all_rows = ROWS_DEV * tok_count
    block_rows = all_rows // BLOCKS
    onehot = (block_order[0][:, None] == jnp.arange(BLOCKS, dtype=jnp.int32)[None, :]).astype(
        jnp.float32
    )
    position = jnp.dot(
        jnp.arange(BLOCKS).astype(jnp.float32), onehot, precision=lax.Precision.HIGHEST
    )
    block_weight = (1.0 - RATE_DECAY) * jnp.power(jnp.float32(RATE_DECAY), BLOCKS - 1.0 - position)
    row_weight = jnp.repeat(block_weight / block_rows, block_rows).reshape(
        tok_count, MICRO, local_rows
    )
    carried = jnp.zeros((local_rows, width), jnp.bfloat16)
    layer_buf = jnp.zeros((ROWS_DEV, width), jnp.bfloat16)
    recon_buf = jnp.zeros((ROWS_DEV, width), jnp.bfloat16)
    latent_buf = jnp.zeros((tok_count, MICRO, local_rows, lat_local), jnp.bfloat16)
    rate_acc = jnp.zeros((lat_local,), jnp.float32)

    def tick_step(tick, state):
        carried, layer_buf, recon_buf, latent_buf, rate_acc = state
        micro_here = tick - segment_index
        valid = jnp.logical_and(micro_here >= 0, micro_here < MICRO)
        micro_idx = jnp.clip(micro_here, 0, MICRO - 1)
        fresh = lax.dynamic_slice_in_dim(
            window, jnp.minimum(tick, MICRO - 1) * local_rows, local_rows, 0
        )
        incoming = jnp.where(segment_index == 0, fresh, carried)
        hidden = incoming.astype(jnp.float32)
        scale = lax.rsqrt(jnp.mean(hidden * hidden, axis=-1, keepdims=True) + EPSILON)
        normed = (hidden * scale * gain_row).astype(jnp.bfloat16)
        pre_act = (
            jnp.dot(
                lax.all_gather(normed, "tok", axis=0, tiled=True),
                encoder,
                preferred_element_type=jnp.float32,
            )
            + enc_row
        )
        fire_gate = jax.nn.sigmoid(SHARPNESS * (pre_act - theta_row))
        latents = (pre_act * fire_gate).astype(jnp.bfloat16)
        weights_now = lax.dynamic_slice(
            row_weight, (0, micro_idx, 0), (tok_count, 1, local_rows)
        ).reshape(-1)
        rate_term = jnp.dot(weights_now, fire_gate, precision=lax.Precision.HIGHEST)
        rate_acc = rate_acc + jnp.where(valid, rate_term, 0.0)
        latent_grid = latents.reshape(tok_count, 1, local_rows, lat_local)
        previous = lax.dynamic_slice(
            latent_buf, (0, micro_idx, 0, 0), (tok_count, 1, local_rows, lat_local)
        )
        latent_buf = lax.dynamic_update_slice(
            latent_buf, jnp.where(valid, latent_grid, previous), (0, micro_idx, 0, 0)
        )
        partial_sum = jnp.dot(latents, decoder, preferred_element_type=jnp.float32)
        mine = reduce_rows(partial_sum, local_rows)
        recon_sum = mine + dec_row
        layer = (hidden + recon_sum).astype(jnp.bfloat16)
        recon_now = recon_sum.astype(jnp.bfloat16)
        row_start = micro_idx * local_rows
        old_layer = lax.dynamic_slice_in_dim(layer_buf, row_start, local_rows, 0)
        layer_buf = lax.dynamic_update_slice_in_dim(
            layer_buf, jnp.where(valid, layer, old_layer), row_start, 0
        )
        old_recon = lax.dynamic_slice_in_dim(recon_buf, row_start, local_rows, 0)
        recon_buf = lax.dynamic_update_slice_in_dim(
            recon_buf, jnp.where(valid, recon_now, old_recon), row_start, 0
        )
        carried = from_behind(layer, "segment", 1)
        return carried, layer_buf, recon_buf, latent_buf, rate_acc

    state = (carried, layer_buf, recon_buf, latent_buf, rate_acc)
    state = lax.fori_loop(0, MICRO + segment_count - 1, tick_step, state)
    carried, layer_buf, recon_buf, latent_buf, rate_acc = state
    final_rates = RATE_DECAY**BLOCKS * rates_start[0] + rate_acc
    latent_out = latent_buf.reshape(tok_count * ROWS_DEV, lat_local)
    return (layer_buf[None], latent_out[None], recon_buf[None], final_rates[None])


def solution(mesh):
    placed = (
        P("tok", None),
        P("segment", None),
        P("segment", None, ("latent", "tok")),
        P("segment", ("latent", "tok")),
        P("segment", ("latent", "tok")),
        P("segment", ("latent", "tok"), None),
        P("segment", None),
        P("segment", ("latent", "tok")),
        P("segment", None),
    )
    return jax.shard_map(
        per_device,
        mesh=mesh,
        in_specs=placed,
        out_specs=(
            P("segment", "tok", None),
            P("segment", None, ("latent", "tok")),
            P("segment", "tok", None),
            P("segment", ("latent", "tok")),
        ),
        check_vma=False,
    )
```

```python
import jax
import jax.numpy as jnp
from jax import lax
from jax.sharding import PartitionSpec as P
from jax.experimental import pallas as pl
from jax.experimental.pallas import tpu as pltpu

ROWS_DEV = 128
CHUNK = 512
MICRO = 4
BLOCKS = 8


EPSILON = 1e-06
SHARPNESS = 20.0
RATE_DECAY = 0.8


def from_behind(array, axis, by):
    devices = lax.axis_size(axis)
    pairs = [(i, i + by) for i in range(devices) if 0 <= i + by < devices]
    return lax.ppermute(array, axis, pairs)


def transcoder_kernel(x_ref, enc_ref, bias_ref, theta_ref, dec_ref, lat_ref, gate_ref, part_ref):
    @pl.when(pl.program_id(0) == 0)
    def _():
        part_ref[...] = jnp.zeros_like(part_ref)

    pre = jnp.dot(x_ref[...], enc_ref[...], preferred_element_type=jnp.float32)
    pre = pre + bias_ref[...]
    gate = jax.nn.sigmoid(SHARPNESS * (pre - theta_ref[...]))
    lat = (pre * gate).astype(jnp.bfloat16)
    lat_ref[...] = lat
    gate_ref[...] = gate
    part_ref[...] += jnp.dot(lat, dec_ref[...], preferred_element_type=jnp.float32)


def transcode(rows, encoder, bias_row, theta_row, decoder):
    count, width = rows.shape
    lat_local = encoder.shape[1]
    return pl.pallas_call(
        transcoder_kernel,
        out_shape=(
            jax.ShapeDtypeStruct((count, lat_local), jnp.bfloat16),
            jax.ShapeDtypeStruct((count, lat_local), jnp.float32),
            jax.ShapeDtypeStruct((count, width), jnp.float32),
        ),
        grid=(lat_local // CHUNK,),
        in_specs=[
            pl.BlockSpec((count, width), lambda c: (0, 0)),
            pl.BlockSpec((width, CHUNK), lambda c: (0, c)),
            pl.BlockSpec((1, CHUNK), lambda c: (0, c)),
            pl.BlockSpec((1, CHUNK), lambda c: (0, c)),
            pl.BlockSpec((CHUNK, width), lambda c: (c, 0)),
        ],
        out_specs=(
            pl.BlockSpec((count, CHUNK), lambda c: (0, c)),
            pl.BlockSpec((count, CHUNK), lambda c: (0, c)),
            pl.BlockSpec((count, width), lambda c: (0, 0)),
        ),
        compiler_params=pltpu.CompilerParams(
            dimension_semantics=("arbitrary",), vmem_limit_bytes=48 * 1024 * 1024
        ),
        cost_estimate=pl.CostEstimate(
            flops=4 * count * width * lat_local,
            transcendentals=count * lat_local,
            bytes_accessed=4 * width * lat_local,
        ),
    )(rows, encoder, bias_row, theta_row, decoder)


def swap_with(array, axis, bit):
    devices = lax.axis_size(axis)
    return lax.ppermute(array, axis, [(i, i ^ bit) for i in range(devices)])


def reduce_rows(partial_sum, local_rows):
    width = partial_sum.shape[1]
    tok_index = lax.axis_index("tok")
    core = tok_index % 2
    low = tok_index // 2
    blocks = partial_sum.reshape(2, 2, local_rows, width)
    keep = lax.dynamic_index_in_dim(blocks, core, axis=1, keepdims=False)
    send = lax.dynamic_index_in_dim(blocks, 1 - core, axis=1, keepdims=False)
    halves = keep + widen(swap_with(send.astype(jnp.bfloat16), "tok", 1))
    keep = lax.dynamic_index_in_dim(halves, low, axis=0, keepdims=False)
    send = lax.dynamic_index_in_dim(halves, 1 - low, axis=0, keepdims=False)
    total = keep + widen(swap_with(send.astype(jnp.bfloat16), "tok", 2))
    for step in range(3):
        narrow = total.astype(jnp.bfloat16)
        total = widen(narrow) + widen(
            lax.ppermute(narrow, ("latent", "tok"), latent_round(step))
        )
    return total


def widen(array):
    return array.astype(jnp.float32)


def latent_round(step):
    orders = ((4, 1, 2), (2, 4, 1))
    pairs = []
    for latent in range(8):
        for tok in range(4):
            bit = orders[tok % 2][step]
            pairs.append((latent * 4 + tok, (latent ^ bit) * 4 + tok))
    return pairs


def per_device(
    window,
    norm_gain,
    enc_weight,
    enc_bias,
    thresholds,
    dec_weight,
    dec_bias,
    rates_start,
    block_order,
):
    tok_count = lax.axis_size("tok")
    my_index = lax.axis_index("tok")
    segment_count = lax.axis_size("segment")
    segment_index = lax.axis_index("segment")
    local_rows = ROWS_DEV // MICRO
    width = window.shape[1]
    encoder = enc_weight[0]
    decoder = dec_weight[0]
    lat_local = encoder.shape[1]
    gain_row = norm_gain[0][None, :]
    enc_row = enc_bias[0][None, :]
    theta_row = thresholds[0].astype(jnp.float32)[None, :] / 1024.0
    dec_row = dec_bias[0][None, :]
    all_rows = ROWS_DEV * tok_count
    block_rows = all_rows // BLOCKS
    onehot = (block_order[0][:, None] == jnp.arange(BLOCKS, dtype=jnp.int32)[None, :]).astype(
        jnp.float32
    )
    position = jnp.dot(
        jnp.arange(BLOCKS).astype(jnp.float32), onehot, precision=lax.Precision.HIGHEST
    )
    block_weight = (1.0 - RATE_DECAY) * jnp.power(jnp.float32(RATE_DECAY), BLOCKS - 1.0 - position)
    row_weight = jnp.repeat(block_weight / block_rows, block_rows).reshape(
        tok_count, MICRO, local_rows
    )
    carried = jnp.zeros((local_rows, width), jnp.bfloat16)
    layer_buf = jnp.zeros((ROWS_DEV, width), jnp.bfloat16)
    recon_buf = jnp.zeros((ROWS_DEV, width), jnp.bfloat16)
    latent_buf = jnp.zeros((tok_count, MICRO, local_rows, lat_local), jnp.bfloat16)
    rate_acc = jnp.zeros((lat_local,), jnp.float32)
    for tick in range(MICRO + segment_count - 1):
        micro_here = tick - segment_index
        valid = jnp.logical_and(micro_here >= 0, micro_here < MICRO)
        micro_idx = jnp.clip(micro_here, 0, MICRO - 1)
        if tick < MICRO:
            fresh = window[tick * local_rows : (tick + 1) * local_rows]
        else:
            fresh = jnp.zeros((local_rows, width), jnp.bfloat16)
        incoming = jnp.where(segment_index == 0, fresh, carried)
        hidden = incoming.astype(jnp.float32)
        scale = lax.rsqrt(jnp.mean(hidden * hidden, axis=-1, keepdims=True) + EPSILON)
        normed = (hidden * scale * gain_row).astype(jnp.bfloat16)
        latents, fire_gate, partial_sum = transcode(
            lax.all_gather(normed, "tok", axis=0, tiled=True),
            encoder,
            enc_row,
            theta_row,
            decoder,
        )
        weights_now = lax.dynamic_slice(
            row_weight, (0, micro_idx, 0), (tok_count, 1, local_rows)
        ).reshape(-1)
        rate_term = jnp.dot(weights_now, fire_gate, precision=lax.Precision.HIGHEST)
        rate_acc = rate_acc + jnp.where(valid, rate_term, 0.0)
        latent_grid = latents.reshape(tok_count, 1, local_rows, lat_local)
        previous = lax.dynamic_slice(
            latent_buf, (0, micro_idx, 0, 0), (tok_count, 1, local_rows, lat_local)
        )
        latent_buf = lax.dynamic_update_slice(
            latent_buf, jnp.where(valid, latent_grid, previous), (0, micro_idx, 0, 0)
        )
        mine = reduce_rows(partial_sum, local_rows)
        recon_sum = mine + dec_row
        layer = (hidden + recon_sum).astype(jnp.bfloat16)
        recon_now = recon_sum.astype(jnp.bfloat16)
        row_start = micro_idx * local_rows
        old_layer = lax.dynamic_slice_in_dim(layer_buf, row_start, local_rows, 0)
        layer_buf = lax.dynamic_update_slice_in_dim(
            layer_buf, jnp.where(valid, layer, old_layer), row_start, 0
        )
        old_recon = lax.dynamic_slice_in_dim(recon_buf, row_start, local_rows, 0)
        recon_buf = lax.dynamic_update_slice_in_dim(
            recon_buf, jnp.where(valid, recon_now, old_recon), row_start, 0
        )
        carried = from_behind(layer, "segment", 1)
    final_rates = RATE_DECAY**BLOCKS * rates_start[0] + rate_acc
    latent_out = latent_buf.reshape(tok_count * ROWS_DEV, lat_local)
    return (layer_buf[None], latent_out[None], recon_buf[None], final_rates[None])


def solution(mesh):
    placed = (
        P("tok", None),
        P("segment", None),
        P("segment", None, ("latent", "tok")),
        P("segment", ("latent", "tok")),
        P("segment", ("latent", "tok")),
        P("segment", ("latent", "tok"), None),
        P("segment", None),
        P("segment", ("latent", "tok")),
        P("segment", None),
    )
    return jax.shard_map(
        per_device,
        mesh=mesh,
        in_specs=placed,
        out_specs=(
            P("segment", "tok", None),
            P("segment", None, ("latent", "tok")),
            P("segment", "tok", None),
            P("segment", ("latent", "tok")),
        ),
        check_vma=False,
    )
```

```python
import jax
import jax.numpy as jnp
from jax import lax
from jax.sharding import PartitionSpec as P

ROWS_DEV = 128
MICRO = 4
BLOCKS = 8


EPSILON = 1e-06
SHARPNESS = 20.0
RATE_DECAY = 0.8


def from_behind(array, axis, by):
    devices = lax.axis_size(axis)
    pairs = [(i, i + by) for i in range(devices) if 0 <= i + by < devices]
    return lax.ppermute(array, axis, pairs)


def swap_with(array, axis, bit):
    devices = lax.axis_size(axis)
    return lax.ppermute(array, axis, [(i, i ^ bit) for i in range(devices)])


def reduce_rows(partial_sum, local_rows):
    width = partial_sum.shape[1]
    tok_index = lax.axis_index("tok")
    core = tok_index % 2
    low = tok_index // 2
    blocks = partial_sum.reshape(2, 2, local_rows, width)
    keep = lax.dynamic_index_in_dim(blocks, core, axis=1, keepdims=False)
    send = lax.dynamic_index_in_dim(blocks, 1 - core, axis=1, keepdims=False)
    halves = keep + widen(swap_with(send.astype(jnp.bfloat16), "tok", 1))
    keep = lax.dynamic_index_in_dim(halves, low, axis=0, keepdims=False)
    send = lax.dynamic_index_in_dim(halves, 1 - low, axis=0, keepdims=False)
    total = keep + widen(swap_with(send.astype(jnp.bfloat16), "tok", 2))
    return spread_over_latent(total)


def spread_over_latent(total):
    count = lax.axis_size("latent")
    rows, width = total.shape
    pieces = total.reshape(count, rows // count, width).astype(jnp.bfloat16)
    arrived = lax.all_to_all(pieces, "latent", 0, 0)
    piece = jnp.sum(widen(arrived), axis=0)
    copies = jnp.broadcast_to(piece[None], (count,) + piece.shape)
    gathered = lax.all_to_all(copies, "latent", 0, 0)
    return gathered.reshape(rows, width)


def widen(array):
    return array.astype(jnp.float32)


def latent_round(step):
    orders = ((4, 1, 2), (2, 4, 1))
    pairs = []
    for latent in range(8):
        for tok in range(4):
            bit = orders[tok % 2][step]
            pairs.append((latent * 4 + tok, (latent ^ bit) * 4 + tok))
    return pairs


def per_device(
    window,
    norm_gain,
    enc_weight,
    enc_bias,
    thresholds,
    dec_weight,
    dec_bias,
    rates_start,
    block_order,
):
    tok_count = lax.axis_size("tok")
    my_index = lax.axis_index("tok")
    segment_count = lax.axis_size("segment")
    segment_index = lax.axis_index("segment")
    local_rows = ROWS_DEV // MICRO
    width = window.shape[1]
    encoder = enc_weight[0]
    decoder = dec_weight[0]
    lat_local = encoder.shape[1]
    gain_row = norm_gain[0][None, :]
    enc_row = enc_bias[0][None, :]
    theta_row = thresholds[0].astype(jnp.float32)[None, :] / 1024.0
    dec_row = dec_bias[0][None, :]
    all_rows = ROWS_DEV * tok_count
    block_rows = all_rows // BLOCKS
    onehot = (block_order[0][:, None] == jnp.arange(BLOCKS, dtype=jnp.int32)[None, :]).astype(
        jnp.float32
    )
    position = jnp.dot(
        jnp.arange(BLOCKS).astype(jnp.float32), onehot, precision=lax.Precision.HIGHEST
    )
    block_weight = (1.0 - RATE_DECAY) * jnp.power(jnp.float32(RATE_DECAY), BLOCKS - 1.0 - position)
    row_weight = jnp.repeat(block_weight / block_rows, block_rows).reshape(
        tok_count, MICRO, local_rows
    )
    carried = jnp.zeros((local_rows, width), jnp.bfloat16)
    layer_buf = jnp.zeros((ROWS_DEV, width), jnp.bfloat16)
    recon_buf = jnp.zeros((ROWS_DEV, width), jnp.bfloat16)
    latent_buf = jnp.zeros((tok_count, MICRO, local_rows, lat_local), jnp.bfloat16)
    rate_acc = jnp.zeros((lat_local,), jnp.float32)
    for tick in range(MICRO + segment_count - 1):
        micro_here = tick - segment_index
        valid = jnp.logical_and(micro_here >= 0, micro_here < MICRO)
        micro_idx = jnp.clip(micro_here, 0, MICRO - 1)
        if tick < MICRO:
            fresh = window[tick * local_rows : (tick + 1) * local_rows]
        else:
            fresh = jnp.zeros((local_rows, width), jnp.bfloat16)
        incoming = jnp.where(segment_index == 0, fresh, carried)
        hidden = incoming.astype(jnp.float32)
        scale = lax.rsqrt(jnp.mean(hidden * hidden, axis=-1, keepdims=True) + EPSILON)
        normed = (hidden * scale * gain_row).astype(jnp.bfloat16)
        pre_act = (
            jnp.dot(
                lax.all_gather(normed, "tok", axis=0, tiled=True),
                encoder,
                preferred_element_type=jnp.float32,
            )
            + enc_row
        )
        fire_gate = jax.nn.sigmoid(SHARPNESS * (pre_act - theta_row))
        latents = (pre_act * fire_gate).astype(jnp.bfloat16)
        weights_now = lax.dynamic_slice(
            row_weight, (0, micro_idx, 0), (tok_count, 1, local_rows)
        ).reshape(-1)
        rate_term = jnp.dot(weights_now, fire_gate, precision=lax.Precision.HIGHEST)
        rate_acc = rate_acc + jnp.where(valid, rate_term, 0.0)
        latent_grid = latents.reshape(tok_count, 1, local_rows, lat_local)
        previous = lax.dynamic_slice(
            latent_buf, (0, micro_idx, 0, 0), (tok_count, 1, local_rows, lat_local)
        )
        latent_buf = lax.dynamic_update_slice(
            latent_buf, jnp.where(valid, latent_grid, previous), (0, micro_idx, 0, 0)
        )
        partial_sum = jnp.dot(latents, decoder, preferred_element_type=jnp.float32)
        mine = reduce_rows(partial_sum, local_rows)
        recon_sum = mine + dec_row
        layer = (hidden + recon_sum).astype(jnp.bfloat16)
        recon_now = recon_sum.astype(jnp.bfloat16)
        row_start = micro_idx * local_rows
        old_layer = lax.dynamic_slice_in_dim(layer_buf, row_start, local_rows, 0)
        layer_buf = lax.dynamic_update_slice_in_dim(
            layer_buf, jnp.where(valid, layer, old_layer), row_start, 0
        )
        old_recon = lax.dynamic_slice_in_dim(recon_buf, row_start, local_rows, 0)
        recon_buf = lax.dynamic_update_slice_in_dim(
            recon_buf, jnp.where(valid, recon_now, old_recon), row_start, 0
        )
        carried = from_behind(layer, "segment", 1)
    final_rates = RATE_DECAY**BLOCKS * rates_start[0] + rate_acc
    latent_out = latent_buf.reshape(tok_count * ROWS_DEV, lat_local)
    return (layer_buf[None], latent_out[None], recon_buf[None], final_rates[None])


def solution(mesh):
    placed = (
        P("tok", None),
        P("segment", None),
        P("segment", None, ("latent", "tok")),
        P("segment", ("latent", "tok")),
        P("segment", ("latent", "tok")),
        P("segment", ("latent", "tok"), None),
        P("segment", None),
        P("segment", ("latent", "tok")),
        P("segment", None),
    )
    return jax.shard_map(
        per_device,
        mesh=mesh,
        in_specs=placed,
        out_specs=(
            P("segment", "tok", None),
            P("segment", None, ("latent", "tok")),
            P("segment", "tok", None),
            P("segment", ("latent", "tok")),
        ),
        check_vma=False,
    )
```

```python
import jax
import jax.numpy as jnp
from jax import lax
from jax.sharding import PartitionSpec as P

ROWS_DEV = 128
MICRO = 4
BLOCKS = 8


EPSILON = 1e-06
SHARPNESS = 20.0
RATE_DECAY = 0.8


def from_behind(array, axis, by):
    devices = lax.axis_size(axis)
    pairs = [(i, i + by) for i in range(devices) if 0 <= i + by < devices]
    return lax.ppermute(array, axis, pairs)


def swap_with(array, axis, bit):
    devices = lax.axis_size(axis)
    return lax.ppermute(array, axis, [(i, i ^ bit) for i in range(devices)])


def reduce_rows(partial_sum, local_rows):
    width = partial_sum.shape[1]
    tok_index = lax.axis_index("tok")
    core = tok_index % 2
    low = tok_index // 2
    blocks = partial_sum.reshape(2, 2, local_rows, width)
    keep = lax.dynamic_index_in_dim(blocks, core, axis=1, keepdims=False)
    send = lax.dynamic_index_in_dim(blocks, 1 - core, axis=1, keepdims=False)
    halves = keep + widen(swap_with(send.astype(jnp.bfloat16), "tok", 1))
    keep = lax.dynamic_index_in_dim(halves, low, axis=0, keepdims=False)
    send = lax.dynamic_index_in_dim(halves, 1 - low, axis=0, keepdims=False)
    total = keep + widen(swap_with(send.astype(jnp.bfloat16), "tok", 2))
    for step in range(3):
        narrow = total.astype(jnp.bfloat16)
        total = widen(narrow) + widen(
            lax.ppermute(narrow, ("latent", "tok"), latent_round(step))
        )
    return total


def widen(array):
    return array.astype(jnp.float32)


def latent_round(step):
    orders = ((4, 1, 2), (4, 1, 2))
    pairs = []
    for latent in range(8):
        for tok in range(4):
            bit = orders[tok % 2][step]
            pairs.append((latent * 4 + tok, (latent ^ bit) * 4 + tok))
    return pairs


def per_device(
    window,
    norm_gain,
    enc_weight,
    enc_bias,
    thresholds,
    dec_weight,
    dec_bias,
    rates_start,
    block_order,
):
    tok_count = lax.axis_size("tok")
    my_index = lax.axis_index("tok")
    segment_count = lax.axis_size("segment")
    segment_index = lax.axis_index("segment")
    local_rows = ROWS_DEV // MICRO
    width = window.shape[1]
    encoder = enc_weight[0]
    decoder = dec_weight[0]
    lat_local = encoder.shape[1]
    gain_row = norm_gain[0][None, :]
    enc_row = enc_bias[0][None, :]
    theta_row = thresholds[0].astype(jnp.float32)[None, :] / 1024.0
    dec_row = dec_bias[0][None, :]
    all_rows = ROWS_DEV * tok_count
    block_rows = all_rows // BLOCKS
    onehot = (block_order[0][:, None] == jnp.arange(BLOCKS, dtype=jnp.int32)[None, :]).astype(
        jnp.float32
    )
    position = jnp.dot(
        jnp.arange(BLOCKS).astype(jnp.float32), onehot, precision=lax.Precision.HIGHEST
    )
    block_weight = (1.0 - RATE_DECAY) * jnp.power(jnp.float32(RATE_DECAY), BLOCKS - 1.0 - position)
    row_weight = jnp.repeat(block_weight / block_rows, block_rows).reshape(
        tok_count, MICRO, local_rows
    )
    carried = jnp.zeros((local_rows, width), jnp.bfloat16)
    layer_buf = jnp.zeros((ROWS_DEV, width), jnp.bfloat16)
    recon_buf = jnp.zeros((ROWS_DEV, width), jnp.bfloat16)
    latent_buf = jnp.zeros((tok_count, MICRO, local_rows, lat_local), jnp.bfloat16)
    rate_acc = jnp.zeros((lat_local,), jnp.float32)
    for tick in range(MICRO + segment_count - 1):
        micro_here = tick - segment_index
        valid = jnp.logical_and(micro_here >= 0, micro_here < MICRO)
        micro_idx = jnp.clip(micro_here, 0, MICRO - 1)
        if tick < MICRO:
            fresh = window[tick * local_rows : (tick + 1) * local_rows]
        else:
            fresh = jnp.zeros((local_rows, width), jnp.bfloat16)
        incoming = jnp.where(segment_index == 0, fresh, carried)
        hidden = incoming.astype(jnp.float32)
        scale = lax.rsqrt(jnp.mean(hidden * hidden, axis=-1, keepdims=True) + EPSILON)
        normed = (hidden * scale * gain_row).astype(jnp.bfloat16)
        pre_act = (
            jnp.dot(
                lax.all_gather(normed, "tok", axis=0, tiled=True),
                encoder,
                preferred_element_type=jnp.float32,
            )
            + enc_row
        )
        fire_gate = jax.nn.sigmoid(SHARPNESS * (pre_act - theta_row))
        latents = (pre_act * fire_gate).astype(jnp.bfloat16)
        weights_now = lax.dynamic_slice(
            row_weight, (0, micro_idx, 0), (tok_count, 1, local_rows)
        ).reshape(-1)
        rate_term = jnp.dot(weights_now, fire_gate, precision=lax.Precision.HIGHEST)
        rate_acc = rate_acc + jnp.where(valid, rate_term, 0.0)
        latent_grid = latents.reshape(tok_count, 1, local_rows, lat_local)
        previous = lax.dynamic_slice(
            latent_buf, (0, micro_idx, 0, 0), (tok_count, 1, local_rows, lat_local)
        )
        latent_buf = lax.dynamic_update_slice(
            latent_buf, jnp.where(valid, latent_grid, previous), (0, micro_idx, 0, 0)
        )
        partial_sum = jnp.dot(latents, decoder, preferred_element_type=jnp.float32)
        mine = reduce_rows(partial_sum, local_rows)
        recon_sum = mine + dec_row
        layer = (hidden + recon_sum).astype(jnp.bfloat16)
        recon_now = recon_sum.astype(jnp.bfloat16)
        row_start = micro_idx * local_rows
        old_layer = lax.dynamic_slice_in_dim(layer_buf, row_start, local_rows, 0)
        layer_buf = lax.dynamic_update_slice_in_dim(
            layer_buf, jnp.where(valid, layer, old_layer), row_start, 0
        )
        old_recon = lax.dynamic_slice_in_dim(recon_buf, row_start, local_rows, 0)
        recon_buf = lax.dynamic_update_slice_in_dim(
            recon_buf, jnp.where(valid, recon_now, old_recon), row_start, 0
        )
        carried = from_behind(layer, "segment", 1)
    final_rates = RATE_DECAY**BLOCKS * rates_start[0] + rate_acc
    latent_out = latent_buf.reshape(tok_count * ROWS_DEV, lat_local)
    return (layer_buf[None], latent_out[None], recon_buf[None], final_rates[None])


def solution(mesh):
    placed = (
        P("tok", None),
        P("segment", None),
        P("segment", None, ("latent", "tok")),
        P("segment", ("latent", "tok")),
        P("segment", ("latent", "tok")),
        P("segment", ("latent", "tok"), None),
        P("segment", None),
        P("segment", ("latent", "tok")),
        P("segment", None),
    )
    return jax.shard_map(
        per_device,
        mesh=mesh,
        in_specs=placed,
        out_specs=(
            P("segment", "tok", None),
            P("segment", None, ("latent", "tok")),
            P("segment", "tok", None),
            P("segment", ("latent", "tok")),
        ),
        check_vma=False,
    )
```

```python
import jax
import jax.numpy as jnp
from jax import lax
from jax.sharding import PartitionSpec as P

ROWS_DEV = 128
MICRO = 4
BLOCKS = 8


EPSILON = 1e-06
SHARPNESS = 20.0
RATE_DECAY = 0.8


def from_behind(array, axis, by):
    devices = lax.axis_size(axis)
    pairs = [(i, i + by) for i in range(devices) if 0 <= i + by < devices]
    return lax.ppermute(array, axis, pairs)


def swap_with(array, axis, bit):
    devices = lax.axis_size(axis)
    return lax.ppermute(array, axis, [(i, i ^ bit) for i in range(devices)])


def reduce_rows(partial_sum, local_rows):
    width = partial_sum.shape[1]
    tok_index = lax.axis_index("tok")
    core = tok_index % 2
    low = tok_index // 2
    blocks = partial_sum.reshape(2, 2, local_rows, width)
    keep = lax.dynamic_index_in_dim(blocks, core, axis=1, keepdims=False)
    send = lax.dynamic_index_in_dim(blocks, 1 - core, axis=1, keepdims=False)
    halves = keep + widen(swap_with(send.astype(jnp.bfloat16), "tok", 1))
    keep = lax.dynamic_index_in_dim(halves, low, axis=0, keepdims=False)
    send = lax.dynamic_index_in_dim(halves, 1 - low, axis=0, keepdims=False)
    total = keep + widen(swap_with(send.astype(jnp.bfloat16), "tok", 2))
    for step in range(3):
        narrow = total.astype(jnp.bfloat16)
        total = widen(narrow) + widen(
            lax.ppermute(narrow, ("latent", "tok"), latent_round(step))
        )
    return total


def widen(array):
    return array.astype(jnp.float32)


def latent_round(step):
    partner = {
        "y": lambda latent: latent ^ 4,
        "a": lambda latent: latent ^ 1,
        "b": lambda latent: (latent & 4) | (3 - (latent & 3)),
    }
    orders = (("y", "a", "b"), ("b", "y", "a"))
    pairs = []
    for latent in range(8):
        for tok in range(4):
            other = partner[orders[tok % 2][step]](latent)
            pairs.append((latent * 4 + tok, other * 4 + tok))
    return pairs


def per_device(
    window,
    norm_gain,
    enc_weight,
    enc_bias,
    thresholds,
    dec_weight,
    dec_bias,
    rates_start,
    block_order,
):
    tok_count = lax.axis_size("tok")
    my_index = lax.axis_index("tok")
    segment_count = lax.axis_size("segment")
    segment_index = lax.axis_index("segment")
    local_rows = ROWS_DEV // MICRO
    width = window.shape[1]
    encoder = enc_weight[0]
    decoder = dec_weight[0]
    lat_local = encoder.shape[1]
    gain_row = norm_gain[0][None, :]
    enc_row = enc_bias[0][None, :]
    theta_row = thresholds[0].astype(jnp.float32)[None, :] / 1024.0
    dec_row = dec_bias[0][None, :]
    all_rows = ROWS_DEV * tok_count
    block_rows = all_rows // BLOCKS
    onehot = (block_order[0][:, None] == jnp.arange(BLOCKS, dtype=jnp.int32)[None, :]).astype(
        jnp.float32
    )
    position = jnp.dot(
        jnp.arange(BLOCKS).astype(jnp.float32), onehot, precision=lax.Precision.HIGHEST
    )
    block_weight = (1.0 - RATE_DECAY) * jnp.power(jnp.float32(RATE_DECAY), BLOCKS - 1.0 - position)
    row_weight = jnp.repeat(block_weight / block_rows, block_rows).reshape(
        tok_count, MICRO, local_rows
    )
    carried = jnp.zeros((local_rows, width), jnp.bfloat16)
    layer_buf = jnp.zeros((ROWS_DEV, width), jnp.bfloat16)
    recon_buf = jnp.zeros((ROWS_DEV, width), jnp.bfloat16)
    latent_buf = jnp.zeros((tok_count, MICRO, local_rows, lat_local), jnp.bfloat16)
    rate_acc = jnp.zeros((lat_local,), jnp.float32)
    for tick in range(MICRO + segment_count - 1):
        micro_here = tick - segment_index
        valid = jnp.logical_and(micro_here >= 0, micro_here < MICRO)
        micro_idx = jnp.clip(micro_here, 0, MICRO - 1)
        if tick < MICRO:
            fresh = window[tick * local_rows : (tick + 1) * local_rows]
        else:
            fresh = jnp.zeros((local_rows, width), jnp.bfloat16)
        incoming = jnp.where(segment_index == 0, fresh, carried)
        hidden = incoming.astype(jnp.float32)
        scale = lax.rsqrt(jnp.mean(hidden * hidden, axis=-1, keepdims=True) + EPSILON)
        normed = (hidden * scale * gain_row).astype(jnp.bfloat16)
        pre_act = (
            jnp.dot(
                lax.all_gather(normed, "tok", axis=0, tiled=True),
                encoder,
                preferred_element_type=jnp.float32,
            )
            + enc_row
        )
        fire_gate = jax.nn.sigmoid(SHARPNESS * (pre_act - theta_row))
        latents = (pre_act * fire_gate).astype(jnp.bfloat16)
        weights_now = lax.dynamic_slice(
            row_weight, (0, micro_idx, 0), (tok_count, 1, local_rows)
        ).reshape(-1)
        rate_term = jnp.dot(weights_now, fire_gate, precision=lax.Precision.HIGHEST)
        rate_acc = rate_acc + jnp.where(valid, rate_term, 0.0)
        latent_grid = latents.reshape(tok_count, 1, local_rows, lat_local)
        previous = lax.dynamic_slice(
            latent_buf, (0, micro_idx, 0, 0), (tok_count, 1, local_rows, lat_local)
        )
        latent_buf = lax.dynamic_update_slice(
            latent_buf, jnp.where(valid, latent_grid, previous), (0, micro_idx, 0, 0)
        )
        partial_sum = jnp.dot(latents, decoder, preferred_element_type=jnp.float32)
        mine = reduce_rows(partial_sum, local_rows)
        recon_sum = mine + dec_row
        layer = (hidden + recon_sum).astype(jnp.bfloat16)
        recon_now = recon_sum.astype(jnp.bfloat16)
        row_start = micro_idx * local_rows
        old_layer = lax.dynamic_slice_in_dim(layer_buf, row_start, local_rows, 0)
        layer_buf = lax.dynamic_update_slice_in_dim(
            layer_buf, jnp.where(valid, layer, old_layer), row_start, 0
        )
        old_recon = lax.dynamic_slice_in_dim(recon_buf, row_start, local_rows, 0)
        recon_buf = lax.dynamic_update_slice_in_dim(
            recon_buf, jnp.where(valid, recon_now, old_recon), row_start, 0
        )
        carried = from_behind(layer, "segment", 1)
    final_rates = RATE_DECAY**BLOCKS * rates_start[0] + rate_acc
    latent_out = latent_buf.reshape(tok_count * ROWS_DEV, lat_local)
    return (layer_buf[None], latent_out[None], recon_buf[None], final_rates[None])


def solution(mesh):
    placed = (
        P("tok", None),
        P("segment", None),
        P("segment", None, ("latent", "tok")),
        P("segment", ("latent", "tok")),
        P("segment", ("latent", "tok")),
        P("segment", ("latent", "tok"), None),
        P("segment", None),
        P("segment", ("latent", "tok")),
        P("segment", None),
    )
    return jax.shard_map(
        per_device,
        mesh=mesh,
        in_specs=placed,
        out_specs=(
            P("segment", "tok", None),
            P("segment", None, ("latent", "tok")),
            P("segment", "tok", None),
            P("segment", ("latent", "tok")),
        ),
        check_vma=False,
    )
```
